512 devices in a mesh: dp: 4 (over y), expert: 128 (over x, z, core).
Axes of the slice: x: 4, y: 4, z: 16, core: 2. Of those that a mesh axis runs over, the one named last changes fastest.
Arguments:
- tokens: bfloat16 [12288, 2048], P(('dp', 'expert')), may hold values from -6 to 6
- cotangent: bfloat16 [12288, 2048], P(('dp', 'expert')), may hold values from -6 to 6
- routes: int32 [12288, 8], P(('dp', 'expert')), may hold values from 0 to 127, all different within a row; in each aligned block of 24 rows (0 to 23, 24 to 47, ...) at most 2 rows name the same one
- gates: bfloat16 [12288, 8], P(('dp', 'expert')), may hold values from 0.029907227 to 0.25
- plan: int32 [128], replicated, may hold values from 0 to 127, as said below
- gate_values: bfloat16 [128, 768, 2048], P('expert', 'dp'), may hold values from -0.125 to 0.125
- up_values: bfloat16 [128, 768, 2048], P('expert', 'dp'), may hold values from -0.125 to 0.125
- down_values: bfloat16 [128, 768, 2048], P('expert', 'dp'), may hold values from -0.21875 to 0.21875
- gate_scales: float32 [128, 12, 16], P('expert', 'dp'), may hold values from 0.5 to 2
- up_scales: float32 [128, 12, 16], P('expert', 'dp'), may hold values from 0.5 to 2
- down_scales: float32 [128, 12, 16], P('expert', 'dp'), may hold values from 0.5 to 2
Outputs:
- token_grads: bfloat16 [12288, 2048], P(('dp', 'expert'))
- gate_grads: bfloat16 [128, 768, 2048], P('expert', 'dp')
- up_grads: bfloat16 [128, 768, 2048], P('expert', 'dp')
- down_grads: bfloat16 [128, 768, 2048], P('expert', 'dp')
The draws below stay inside these ranges and needn't reach their ends.
Inputs may be any that keep to these rules, and one draw needn't show every extreme that they name: `routes`: each token names 8 different experts. Among the 24 tokens of one device no expert is named more than 2 times, and in every draw the tokens of some device name some expert exactly 2 times. plan[plan[s]] = s, and plan[s] is either s or (s + 64) % 128; plan[0] = 64.
All inputs are finite; a program needn't handle non-finite values.
Results may differ from the reference program's by a relative error of at most 0.0082.
Values may be sent and summed in bfloat16 or wider, within the bound.
No kernel may reach another device: no remote copies, remote signals or barrier semaphores. Data moves between devices by JAX's collectives and lax.ppermute only.
A program may use at most 128 MiB of HBM per device.

```python
import math
import jax
import jax.numpy as jnp
import numpy as np
from jax import lax

D = 2048
FF = 768
TOPK = 8
BLOCK_ROWS = 128
BLOCK_COLS = 64
TOK_DEV = 24
EXPERTS = 128
TOKENS = 12288
CAP = 2
ROWS = 1024
N_DP = 4


def draw_plan(key, part):
    half_count = EXPERTS // 2
    flags = jax.random.randint(key, (half_count,), 0, 2).astype(jnp.int32)
    flags = flags.at[0].set(1)
    slots = jnp.arange(EXPERTS, dtype=jnp.int32)
    partner = (slots + half_count) % EXPERTS
    doubled = jnp.concatenate([flags, flags])
    return jnp.where(doubled == 1, partner, slots).astype(jnp.int32)


def block_scale(own_key, dims, split, low, largest):
    factor_of, own = 1.0, jax.random.fold_in(own_key, 6)
    for dim, blocks in split:
        steps = jnp.exp(jax.random.uniform(jax.random.fold_in(own, dim), (blocks,), jnp.float32, low / len(split), largest / len(split)))
        factor_of = factor_of * jnp.repeat(steps, dims[dim] // blocks).reshape([-1 if axis == dim else 1 for axis in range(len(dims))])
    return factor_of


def shared_out(own_key, own, number, rows, amount, top, limit, skew):
    sequence = jax.random.permutation(own_key, amount)
    heavy_load, common = shares(amount, rows * top, limit, skew, True), shares(amount, rows * top, limit, skew, False)
    places = jnp.arange(amount)

    def named(lengths, rotation):
        used = int((lengths > 0).sum())
        fixed = max(1, used // 4)
        shifted = fixed + (places - fixed + rotation * (used - fixed)) % max(1, amount - fixed)
        return jnp.zeros((amount,), jnp.int32).at[sequence[jnp.where(places < fixed, places, shifted)]].set(jnp.asarray(lengths, jnp.int32))

    lengths = jnp.where(number % 4 == 0, named(heavy_load, number // 4), named(common, number - number // 4 - 1))
    mixed = jax.random.permutation(jax.random.fold_in(own, 3), amount)
    source_of, receiver = mixed[0:amount // 2 * 2:2], mixed[1:amount // 2 * 2:2]
    room = jnp.minimum(lengths[source_of] - 1, limit - lengths[receiver]) // 2
    room = jnp.where((source_of == sequence[0]) | (receiver == sequence[0]) | (lengths[receiver] == 0), 0, jnp.maximum(room, 0))
    shifted = jax.random.randint(jax.random.fold_in(own, 4), (amount // 2,), 0, 1 << 20) % (room + 1)
    lengths = lengths.at[source_of].add(-shifted).at[receiver].add(shifted)
    items = jnp.searchsorted(jnp.cumsum(lengths), jnp.arange(rows * top), side="right").astype(jnp.int32)
    table = items.reshape(top, rows).T
    table = table[jax.random.permutation(jax.random.fold_in(own, 1), rows)]
    rotation = jax.random.randint(jax.random.fold_in(own, 2), (rows, 1), 0, top)
    return jnp.take_along_axis(table, (jnp.arange(top)[None, :] + rotation) % top, axis=1)


def shares(number_of, total, bound, slope, full):
    weights = [(1 << 20) // math.isqrt(grade ** slope) + 1 for grade in range(1, number_of + 1)]
    largest = bound if full else min(bound, max(-(-total // number_of), total * weights[0] // sum(weights)))
    least = 1 if total - largest >= number_of - 1 else 0
    holding, spare = [largest] + [least] * (number_of - 1), total - largest - least * (number_of - 1)
    while spare > 0:
        movable = [i for i in range(1, number_of) if holding[i] < largest] or [i for i in range(1, number_of) if holding[i] < bound]
        whole, remaining = sum([weights[i] for i in movable]), spare
        for i in movable:
            extra = min(bound - holding[i], max(1, remaining * weights[i] // whole), spare)
            holding[i] = holding[i] + extra
            spare = spare - extra
    return np.array(holding)


def noise(stream_key, shape, width, limit, split=(), held_as=jnp.bfloat16):
    entries = jax.random.normal(stream_key, shape, jnp.float32) * width
    if len(split) > 0:
        entries = block_scale(stream_key, shape, split, -0.22, 0.18) * entries
    return jnp.clip(entries, min=-limit, max=limit).astype(held_as)


def setup_inputs(seed: int = 0) -> dict:
    keys = jax.random.split(jax.random.key(seed), 12)
    tokens = noise(keys[0], (TOKENS, D), 1.0, 6.0, ((0, 512),))
    cotangent = noise(keys[1], (TOKENS, D), 1.0, 6.0, ((0, 512),))
    routes_keys = jax.random.split(jax.random.fold_in(keys[2], 1), TOKENS // TOK_DEV)
    routes_turns = jax.random.permutation(jax.random.fold_in(keys[2], 3), TOKENS // TOK_DEV)
    routes = jax.vmap(lambda own, number: shared_out(jax.random.fold_in(keys[2], 2), own, number, TOK_DEV, EXPERTS, TOPK, CAP, 2))(routes_keys, routes_turns).reshape((TOKENS, TOPK))
    gates = jnp.clip(0.029907227 + 0.22009277 * jax.random.uniform(keys[3], (TOKENS, TOPK), jnp.float32) ** block_scale(keys[3], (TOKENS, TOPK), ((0, 512),), -0.2, 0.2), 0.029907227, 0.25).astype(jnp.bfloat16)
    plan = draw_plan(jax.random.fold_in(keys[11], 71), 0)
    gate_values = noise(keys[5], (EXPERTS, FF, D), D ** -0.5, 0.125, ((0, 128), (1, 4)))
    up_values = noise(keys[6], (EXPERTS, FF, D), D ** -0.5, 0.125, ((0, 128), (1, 4)))
    down_values = noise(keys[7], (EXPERTS, FF, D), FF ** -0.5, 0.21875, ((0, 128), (1, 4)))
    gate_scales = jnp.clip(jnp.exp(math.log(2.0) - 1.3862944 * jax.random.uniform(keys[8], (EXPERTS, FF // BLOCK_COLS, D // BLOCK_ROWS), jnp.float32) ** block_scale(keys[8], (EXPERTS, FF // BLOCK_COLS, D // BLOCK_ROWS), ((0, 128), (1, 4)), -0.2, 0.2)), 0.5, 2.0)
    up_scales = jnp.clip(jnp.exp(math.log(2.0) - 1.3862944 * jax.random.uniform(keys[9], (EXPERTS, FF // BLOCK_COLS, D // BLOCK_ROWS), jnp.float32) ** block_scale(keys[9], (EXPERTS, FF // BLOCK_COLS, D // BLOCK_ROWS), ((0, 128), (1, 4)), -0.2, 0.2)), 0.5, 2.0)
    down_scales = jnp.clip(jnp.exp(math.log(2.0) - 1.3862944 * jax.random.uniform(keys[10], (EXPERTS, FF // BLOCK_COLS, D // BLOCK_ROWS), jnp.float32) ** block_scale(keys[10], (EXPERTS, FF // BLOCK_COLS, D // BLOCK_ROWS), ((0, 128), (1, 4)), -0.2, 0.2)), 0.5, 2.0)
    return dict(tokens=tokens, cotangent=cotangent, routes=routes, gates=gates, plan=plan, gate_values=gate_values, up_values=up_values, down_values=down_values, gate_scales=gate_scales, up_scales=up_scales, down_scales=down_scales)


def dequantize(values, scales):
    row_block = values.shape[0] // scales.shape[0]
    col_block = values.shape[1] // scales.shape[1]
    spread = jnp.repeat(jnp.repeat(scales, row_block, axis=0), col_block, axis=1)
    return (values.astype(jnp.float32) * spread).astype(jnp.bfloat16)


def reference(tokens, cotangent, routes, gates, plan, gate_values, up_values, down_values, gate_scales, up_scales, down_scales):
    pair_count = TOKENS * TOPK
    flat_routes = routes.reshape(-1)
    padded_tokens = jnp.concatenate([tokens, jnp.zeros((1, D), jnp.bfloat16)], axis=0)
    padded_cot = jnp.concatenate([cotangent, jnp.zeros((1, D), jnp.bfloat16)], axis=0)
    padded_gates = jnp.concatenate([gates.reshape(-1), jnp.zeros((1,), jnp.bfloat16)], axis=0)
    quarter = FF // N_DP

    def per_expert(running, expert):
        chosen = jnp.nonzero(flat_routes == expert, size=ROWS, fill_value=pair_count)[0].astype(jnp.int32)
        token_of = (chosen // TOPK).astype(jnp.int32)
        token_rows = padded_tokens[token_of]
        gate_rows = padded_gates[chosen]
        cot_rows = (gate_rows.astype(jnp.float32)[:, None] * padded_cot[token_of].astype(jnp.float32)).astype(jnp.bfloat16)
        w_gate = dequantize(gate_values[expert], gate_scales[expert])
        w_up = dequantize(up_values[expert], up_scales[expert])
        w_down = dequantize(down_values[expert], down_scales[expert])
        pre_gate = jnp.dot(token_rows, w_gate.T, preferred_element_type=jnp.float32)
        pre_up = jnp.dot(token_rows, w_up.T, preferred_element_type=jnp.float32)
        sigmoid_gate = jax.nn.sigmoid(pre_gate)
        activated = pre_gate * sigmoid_gate
        hidden = (activated * pre_up).astype(jnp.bfloat16)
        grad_hidden = jnp.dot(cot_rows, w_down.T, preferred_element_type=jnp.float32)
        grad_gate = (grad_hidden * pre_up * sigmoid_gate * (1.0 + pre_gate * (1.0 - sigmoid_gate))).astype(jnp.bfloat16)
        grad_up = (grad_hidden * activated).astype(jnp.bfloat16)
        gate_grad = jnp.dot(grad_gate.T, token_rows, preferred_element_type=jnp.float32).astype(jnp.bfloat16)
        up_grad = jnp.dot(grad_up.T, token_rows, preferred_element_type=jnp.float32).astype(jnp.bfloat16)
        down_grad = jnp.dot(hidden.T, cot_rows, preferred_element_type=jnp.float32).astype(jnp.bfloat16)
        summed = jnp.zeros((ROWS, D), jnp.float32)
        for block_index in range(N_DP):
            columns = slice(block_index * quarter, (block_index + 1) * quarter)
            quarter_piece = jnp.dot(grad_gate[:, columns], w_gate[columns, :], preferred_element_type=jnp.float32)
            quarter_piece = quarter_piece + jnp.dot(grad_up[:, columns], w_up[columns, :], preferred_element_type=jnp.float32)
            summed = summed + lax.optimization_barrier(quarter_piece.astype(jnp.bfloat16)).astype(jnp.float32)
        running = running.at[token_of].add(summed, mode="drop")
        return running, (gate_grad, up_grad, down_grad)

    token_sum, stacked = lax.scan(per_expert, jnp.zeros((TOKENS, D), jnp.float32), jnp.arange(EXPERTS, dtype=jnp.int32))
    gate_all, up_all, down_all = stacked
    return (token_sum.astype(jnp.bfloat16), jnp.take(gate_all, plan, axis=0), jnp.take(up_all, plan, axis=0), jnp.take(down_all, plan, axis=0))
```

```python
import jax
import jax.numpy as jnp
from jax import lax
from jax.sharding import PartitionSpec as P


def swapped(block, axis, stride):
    count = lax.axis_size(axis)
    route = []
    for low in range(count):
        high = low | 1 << stride
        if high != low and high < count:
            route += [(low, high), (high, low)]
    return lax.ppermute(block, axis, route)


def dequantize(values, scales):
    row_block = values.shape[0] // scales.shape[0]
    col_block = values.shape[1] // scales.shape[1]
    spread = jnp.repeat(jnp.repeat(scales, row_block, axis=0), col_block, axis=1)
    return (values.astype(jnp.float32) * spread).astype(jnp.bfloat16)


def slot_choice(route_lists, experts, capacity):
    numbers = jnp.arange(experts, dtype=jnp.int32)
    flattened = route_lists.reshape(-1)
    marked = (flattened[:, None] == numbers).astype(jnp.int32)
    slot_index = jnp.sum((jnp.cumsum(marked, axis=0) - 1) * marked, axis=-1)
    position = flattened * capacity + slot_index
    selected = position[:, None] == jnp.arange(experts * capacity, dtype=jnp.int32)
    return selected.reshape(route_lists.shape + (experts * capacity,))


def contract(left, right, left_dim, right_dim):
    return lax.dot_general(
        left, right, (((left_dim,), (right_dim,)), ((), ())), preferred_element_type=jnp.float32
    )


def expert_work(token_rows, cot_rows, w_gate, w_up, w_down):
    pre_gate = contract(token_rows, w_gate, 1, 1)
    pre_up = contract(token_rows, w_up, 1, 1)
    sigmoid_gate = jax.nn.sigmoid(pre_gate)
    activated = pre_gate * sigmoid_gate
    hidden = (activated * pre_up).astype(jnp.bfloat16)
    grad_hidden = contract(cot_rows, w_down, 1, 1)
    grad_gate = (
        grad_hidden * pre_up * sigmoid_gate * (1.0 + pre_gate * (1.0 - sigmoid_gate))
    ).astype(jnp.bfloat16)
    grad_up = (grad_hidden * activated).astype(jnp.bfloat16)
    gate_grad = contract(grad_gate, token_rows, 0, 0).astype(jnp.bfloat16)
    up_grad = contract(grad_up, token_rows, 0, 0).astype(jnp.bfloat16)
    down_grad = contract(hidden, cot_rows, 0, 0).astype(jnp.bfloat16)
    row_grads = (
        jnp.dot(grad_gate, w_gate, preferred_element_type=jnp.float32)
        + jnp.dot(grad_up, w_up, preferred_element_type=jnp.float32)
    ).astype(jnp.bfloat16)
    return (row_grads, gate_grad, up_grad, down_grad)


def on_device(
    tokens,
    cotangent,
    routes,
    gates,
    plan,
    gate_values,
    up_values,
    down_values,
    gate_scales,
    up_scales,
    down_scales,
):
    tok_count, features = tokens.shape
    experts = lax.axis_size("expert")
    replicas = lax.axis_size("dp")
    capacity = 2
    half_bit = experts.bit_length() - 2
    expert_index = lax.axis_index("expert")
    numbers = jnp.arange(experts, dtype=jnp.int32)
    is_moved = jnp.sum(jnp.where(numbers == expert_index, plan, 0)) != expert_index
    w_gate = dequantize(gate_values[0], gate_scales[0])
    w_up = dequantize(up_values[0], up_scales[0])
    w_down = dequantize(down_values[0], down_scales[0])
    selected = slot_choice(routes, experts, capacity)
    dispatch = jnp.sum(selected.astype(jnp.int32), axis=1).reshape(
        tok_count, experts, capacity
    ).astype(jnp.bfloat16)
    outgoing = jnp.einsum(
        "rec,rd->ecd", dispatch, tokens, preferred_element_type=jnp.float32
    ).astype(jnp.bfloat16)
    slot_gate = jnp.einsum(
        "rkx,rk->x", selected.astype(jnp.float32), gates.astype(jnp.float32)
    ).reshape(experts, capacity)
    lifted = jnp.einsum("rec,rd->ecd", dispatch, cotangent, preferred_element_type=jnp.float32)
    cot_out = (lifted * slot_gate[..., None]).astype(jnp.bfloat16)
    both = jnp.stack([outgoing, cot_out], axis=0)
    arrived = lax.all_to_all(both, "expert", split_axis=1, concat_axis=1, tiled=True)
    gathered = lax.all_gather(arrived, "dp", axis=1, tiled=True)
    token_rows = gathered[0].reshape(-1, features)
    cot_rows = gathered[1].reshape(-1, features)
    row_grads, gate_grad, up_grad, down_grad = expert_work(
        token_rows, cot_rows, w_gate, w_up, w_down
    )
    summed_rows = lax.psum_scatter(
        row_grads.reshape(replicas, experts, capacity, features), "dp", scatter_dimension=0, tiled=True
    )
    returned = lax.all_to_all(summed_rows[0], "expert", split_axis=0, concat_axis=0, tiled=True)
    token_grads = jnp.einsum(
        "rec,ecd->rd", dispatch, returned, preferred_element_type=jnp.float32
    ).astype(jnp.bfloat16)
    arrived_grads = swapped((gate_grad, up_grad, down_grad), "expert", half_bit)
    gate_grad = jnp.where(is_moved, arrived_grads[0], gate_grad)
    up_grad = jnp.where(is_moved, arrived_grads[1], up_grad)
    down_grad = jnp.where(is_moved, arrived_grads[2], down_grad)
    return (token_grads, gate_grad[None], up_grad[None], down_grad[None])


def solution(mesh):
    return jax.shard_map(
        on_device,
        mesh=mesh,
        in_specs=(
            P(("dp", "expert"), None),
            P(("dp", "expert"), None),
            P(("dp", "expert"), None),
            P(("dp", "expert"), None),
            P(),
            P("expert", "dp", None),
            P("expert", "dp", None),
            P("expert", "dp", None),
            P("expert", "dp", None),
            P("expert", "dp", None),
            P("expert", "dp", None),
        ),
        out_specs=(
            P(("dp", "expert"), None),
            P("expert", "dp", None),
            P("expert", "dp", None),
            P("expert", "dp", None),
        ),
        check_vma=False,
    )
```

```python
import jax
import jax.numpy as jnp
from jax import lax
from jax.sharding import PartitionSpec as P


def swapped(block, axis, stride):
    count = lax.axis_size(axis)
    route = []
    for low in range(count):
        high = low | 1 << stride
        if high != low and high < count:
            route += [(low, high), (high, low)]
    return lax.ppermute(block, axis, route)


def dequantize(values, scales):
    row_block = values.shape[0] // scales.shape[0]
    col_block = values.shape[1] // scales.shape[1]
    spread = jnp.repeat(jnp.repeat(scales, row_block, axis=0), col_block, axis=1)
    return (values.astype(jnp.float32) * spread).astype(jnp.bfloat16)


def slot_choice(route_lists, experts, capacity):
    numbers = jnp.arange(experts, dtype=jnp.int32)
    flattened = route_lists.reshape(-1)
    marked = (flattened[:, None] == numbers).astype(jnp.int32)
    slot_index = jnp.sum((jnp.cumsum(marked, axis=0) - 1) * marked, axis=-1)
    position = flattened * capacity + slot_index
    selected = position[:, None] == jnp.arange(experts * capacity, dtype=jnp.int32)
    return selected.reshape(route_lists.shape + (experts * capacity,))


def contract(left, right, left_dim, right_dim):
    return lax.dot_general(
        left, right, (((left_dim,), (right_dim,)), ((), ())), preferred_element_type=jnp.float32
    )


def expert_work(token_rows, cot_rows, w_gate, w_up, w_down):
    pre_gate = contract(token_rows, w_gate, 1, 1)
    pre_up = contract(token_rows, w_up, 1, 1)
    sigmoid_gate = jax.nn.sigmoid(pre_gate)
    activated = pre_gate * sigmoid_gate
    hidden = (activated * pre_up).astype(jnp.bfloat16)
    grad_hidden = contract(cot_rows, w_down, 1, 1)
    grad_gate = (
        grad_hidden * pre_up * sigmoid_gate * (1.0 + pre_gate * (1.0 - sigmoid_gate))
    ).astype(jnp.bfloat16)
    grad_up = (grad_hidden * activated).astype(jnp.bfloat16)
    gate_grad = contract(grad_gate, token_rows, 0, 0)
    up_grad = contract(grad_up, token_rows, 0, 0)
    down_grad = contract(hidden, cot_rows, 0, 0)
    row_grads = (
        jnp.dot(grad_gate, w_gate, preferred_element_type=jnp.float32)
        + jnp.dot(grad_up, w_up, preferred_element_type=jnp.float32)
    ).astype(jnp.bfloat16)
    return (row_grads, gate_grad, up_grad, down_grad)


def on_device(
    tokens,
    cotangent,
    routes,
    gates,
    plan,
    gate_values,
    up_values,
    down_values,
    gate_scales,
    up_scales,
    down_scales,
):
    tok_count, features = tokens.shape
    experts = lax.axis_size("expert")
    replicas = lax.axis_size("dp")
    capacity = 2
    half_bit = experts.bit_length() - 2
    expert_index = lax.axis_index("expert")
    numbers = jnp.arange(experts, dtype=jnp.int32)
    is_moved = jnp.sum(jnp.where(numbers == expert_index, plan, 0)) != expert_index
    own = (
        jnp.concatenate([gate_values, up_values, down_values], axis=0),
        jnp.concatenate([gate_scales, up_scales, down_scales], axis=0),
    )
    partner = swapped(own, "expert", half_bit)
    values, scales = (jnp.where(is_moved, b, a) for a, b in zip(own, partner))
    w_gate, w_up, w_down = (dequantize(values[i], scales[i]) for i in range(3))
    destination = jnp.take(plan, routes, axis=0)
    selected = slot_choice(destination, experts, capacity)
    dispatch = jnp.sum(selected.astype(jnp.int32), axis=1).reshape(
        tok_count, experts, capacity
    ).astype(jnp.bfloat16)
    outgoing = jnp.einsum(
        "rec,rd->ecd", dispatch, tokens, preferred_element_type=jnp.float32
    ).astype(jnp.bfloat16)
    slot_gate = jnp.einsum(
        "rkx,rk->x", selected.astype(jnp.float32), gates.astype(jnp.float32)
    ).reshape(experts, capacity)
    lifted = jnp.einsum("rec,rd->ecd", dispatch, cotangent, preferred_element_type=jnp.float32)
    cot_out = (lifted * slot_gate[..., None]).astype(jnp.bfloat16)
    token_sum = jnp.zeros((tok_count, features), jnp.float32)
    sums = None
    for chunk in range(capacity):
        both = jnp.stack([outgoing[:, chunk], cot_out[:, chunk]], axis=0)
        arrived = lax.all_to_all(both, "expert", split_axis=1, concat_axis=1, tiled=True)
        gathered = lax.all_gather(arrived, "dp", axis=1, tiled=True)
        row_grads, gate_grad, up_grad, down_grad = expert_work(
            gathered[0], gathered[1], w_gate, w_up, w_down
        )
        part = (gate_grad, up_grad, down_grad)
        sums = part if sums is None else tuple(a + b for a, b in zip(sums, part))
        summed_rows = lax.psum_scatter(
            row_grads.reshape(replicas, experts, features), "dp", scatter_dimension=0, tiled=True
        )
        returned = lax.all_to_all(summed_rows[0], "expert", split_axis=0, concat_axis=0, tiled=True)
        token_sum = token_sum + jnp.einsum(
            "re,ed->rd", dispatch[:, :, chunk], returned, preferred_element_type=jnp.float32
        )
    token_grads = token_sum.astype(jnp.bfloat16)
    gate_grad, up_grad, down_grad = (x.astype(jnp.bfloat16) for x in sums)
    return (token_grads, gate_grad[None], up_grad[None], down_grad[None])


def solution(mesh):
    return jax.shard_map(
        on_device,
        mesh=mesh,
        in_specs=(
            P(("dp", "expert"), None),
            P(("dp", "expert"), None),
            P(("dp", "expert"), None),
            P(("dp", "expert"), None),
            P(),
            P("expert", "dp", None),
            P("expert", "dp", None),
            P("expert", "dp", None),
            P("expert", "dp", None),
            P("expert", "dp", None),
            P("expert", "dp", None),
        ),
        out_specs=(
            P(("dp", "expert"), None),
            P("expert", "dp", None),
            P("expert", "dp", None),
            P("expert", "dp", None),
        ),
        check_vma=False,
    )
```

```python
import jax
import jax.numpy as jnp
import numpy as np
from jax import lax
from jax.sharding import Mesh
from jax.sharding import PartitionSpec as P

EXPERT_AXES = ("ex", "ez", "ec")
RING_AXES = ("ez", "ec")


def swapped(block, axis, count, stride):
    route = []
    for low in range(count):
        high = low | 1 << stride
        if high != low and high < count:
            route += [(low, high), (high, low)]
    return lax.ppermute(block, axis, route)


def dequantize(values, scales):
    row_block = values.shape[0] // scales.shape[0]
    col_block = values.shape[1] // scales.shape[1]
    spread = jnp.repeat(jnp.repeat(scales, row_block, axis=0), col_block, axis=1)
    return (values.astype(jnp.float32) * spread).astype(jnp.bfloat16)


def slot_position(route_lists, experts, capacity):
    numbers = jnp.arange(experts, dtype=jnp.int32)
    flattened = route_lists.reshape(-1)
    marked = (flattened[:, None] == numbers).astype(jnp.int32)
    slot_index = jnp.sum((jnp.cumsum(marked, axis=0) - 1) * marked, axis=-1)
    return (flattened * capacity + slot_index).reshape(route_lists.shape)


def contract(left, right, left_dim, right_dim):
    return lax.dot_general(
        left, right, (((left_dim,), (right_dim,)), ((), ())), preferred_element_type=jnp.float32
    )


def expert_work(token_rows, cot_rows, w_gate, w_up, w_down):
    pre_gate = contract(token_rows, w_gate, 1, 1)
    pre_up = contract(token_rows, w_up, 1, 1)
    sigmoid_gate = jax.nn.sigmoid(pre_gate)
    activated = pre_gate * sigmoid_gate
    hidden = (activated * pre_up).astype(jnp.bfloat16)
    grad_hidden = contract(cot_rows, w_down, 1, 1)
    grad_gate = (
        grad_hidden * pre_up * sigmoid_gate * (1.0 + pre_gate * (1.0 - sigmoid_gate))
    ).astype(jnp.bfloat16)
    grad_up = (grad_hidden * activated).astype(jnp.bfloat16)
    gate_grad = contract(grad_gate, token_rows, 0, 0)
    up_grad = contract(grad_up, token_rows, 0, 0)
    down_grad = contract(hidden, cot_rows, 0, 0)
    row_grads = (
        jnp.dot(grad_gate, w_gate, preferred_element_type=jnp.float32)
        + jnp.dot(grad_up, w_up, preferred_element_type=jnp.float32)
    ).astype(jnp.bfloat16)
    return (row_grads, gate_grad, up_grad, down_grad)


def on_device(
    tokens,
    cotangent,
    routes,
    gates,
    plan,
    gate_values,
    up_values,
    down_values,
    gate_scales,
    up_scales,
    down_scales,
):
    tok_count, features = tokens.shape
    n_x, n_z, n_c = (lax.axis_size(a) for a in EXPERT_AXES)
    ring = n_z * n_c
    experts = n_x * ring
    replicas = lax.axis_size("dp")
    capacity = 2
    half_bit = experts.bit_length() - 2
    ring_index = lax.axis_index("ez") * n_c + lax.axis_index("ec")
    expert_index = lax.axis_index("ex") * ring + ring_index
    numbers = jnp.arange(experts, dtype=jnp.int32)
    is_moved = jnp.sum(jnp.where(numbers == expert_index, plan, 0)) != expert_index
    own = (
        jnp.concatenate([gate_values, up_values, down_values], axis=0),
        jnp.concatenate([gate_scales, up_scales, down_scales], axis=0),
    )
    partner = swapped(own, EXPERT_AXES, experts, half_bit)
    values, scales = (jnp.where(is_moved, b, a) for a, b in zip(own, partner))
    w_gate, w_up, w_down = (dequantize(values[i], scales[i]) for i in range(3))

    destination = jnp.take(plan, routes, axis=0)
    position = slot_position(destination, experts, capacity)
    slots = jnp.arange(experts * capacity, dtype=jnp.int32)
    dispatch = jnp.any(position[..., None] == slots, axis=1).astype(jnp.bfloat16).reshape(
        tok_count, experts, capacity
    )
    ring_rows = lax.all_gather(
        jnp.concatenate([tokens, cotangent], axis=1), RING_AXES, axis=0, tiled=True
    )
    ring_position = lax.all_gather(position, RING_AXES, axis=0, tiled=True)
    ring_gates = lax.all_gather(gates, RING_AXES, axis=0, tiled=True)
    target = (
        (jnp.arange(n_x, dtype=jnp.int32)[:, None] * ring + ring_index) * capacity
        + jnp.arange(capacity, dtype=jnp.int32)
    )
    match = ring_position[:, :, None, None] == target
    picked = jnp.any(match, axis=1).astype(jnp.bfloat16).reshape(ring, tok_count, n_x, capacity)
    picked_gate = jnp.sum(
        jnp.where(match, ring_gates[:, :, None, None], jnp.zeros((), ring_gates.dtype)), axis=1
    ).reshape(ring, tok_count, n_x, capacity)
    ring_rows = ring_rows.reshape(ring, tok_count, 2 * features)
    relay_tok = jnp.einsum(
        "srxc,srd->cxsd", picked, ring_rows[:, :, :features], preferred_element_type=jnp.float32
    ).astype(jnp.bfloat16)
    relay_cot = jnp.einsum(
        "srxc,srd->cxsd", picked_gate, ring_rows[:, :, features:], preferred_element_type=jnp.float32
    ).astype(jnp.bfloat16)

    token_sum = jnp.zeros((tok_count, features), jnp.float32)
    sums = None
    for chunk in range(capacity):
        both = jnp.stack([relay_tok[chunk], relay_cot[chunk]], axis=0)
        arrived = lax.all_to_all(both, "ex", split_axis=1, concat_axis=1, tiled=True)
        arrived = arrived.reshape(2, experts, features)
        gathered = lax.all_gather(arrived, "dp", axis=1, tiled=True)
        row_grads, gate_grad, up_grad, down_grad = expert_work(
            gathered[0], gathered[1], w_gate, w_up, w_down
        )
        part = (gate_grad, up_grad, down_grad)
        sums = part if sums is None else tuple(a + b for a, b in zip(sums, part))
        summed_rows = lax.psum_scatter(
            row_grads.reshape(replicas, experts, features), "dp", scatter_dimension=0, tiled=True
        )
        returned = lax.all_to_all(summed_rows[0], EXPERT_AXES, split_axis=0, concat_axis=0, tiled=True)
        token_sum = token_sum + jnp.einsum(
            "re,ed->rd", dispatch[:, :, chunk], returned, preferred_element_type=jnp.float32
        )
    token_grads = token_sum.astype(jnp.bfloat16)
    gate_grad, up_grad, down_grad = (x.astype(jnp.bfloat16) for x in sums)
    return (token_grads, gate_grad[None], up_grad[None], down_grad[None])


def split_mesh(mesh):
    devices = mesh.devices
    flat = devices.reshape(-1)
    sizes = []
    for pick in (lambda d: d.coords[0], lambda d: d.coords[2], lambda d: d.core_on_chip):
        sizes.append(len({pick(d) for d in devices[0]}))
    assert int(np.prod(sizes)) == devices.shape[1]
    return Mesh(flat.reshape((devices.shape[0], *sizes)), ("dp", *EXPERT_AXES))


def solution(mesh):
    fine = split_mesh(mesh)
    rows = P(("dp", *EXPERT_AXES), None)
    weights = P(EXPERT_AXES, "dp", None)
    return jax.shard_map(
        on_device,
        mesh=fine,
        in_specs=(rows, rows, rows, rows, P(), weights, weights, weights, weights, weights, weights),
        out_specs=(rows, weights, weights, weights),
        check_vma=False,
    )
```

```python
import jax
import jax.numpy as jnp
import numpy as np
from jax import lax
from jax.sharding import Mesh
from jax.sharding import PartitionSpec as P

EXPERT_AXES = ("ex", "ez", "ec")


def swapped(block, axis, count, stride):
    route = []
    for low in range(count):
        high = low | 1 << stride
        if high != low and high < count:
            route += [(low, high), (high, low)]
    return lax.ppermute(block, axis, route)


def dequantize(values, scales):
    row_block = values.shape[0] // scales.shape[0]
    col_block = values.shape[1] // scales.shape[1]
    spread = jnp.repeat(jnp.repeat(scales, row_block, axis=0), col_block, axis=1)
    return (values.astype(jnp.float32) * spread).astype(jnp.bfloat16)


def slot_position(route_lists, experts, capacity):
    numbers = jnp.arange(experts, dtype=jnp.int32)
    flattened = route_lists.reshape(-1)
    marked = (flattened[:, None] == numbers).astype(jnp.int32)
    slot_index = jnp.sum((jnp.cumsum(marked, axis=0) - 1) * marked, axis=-1)
    return (flattened * capacity + slot_index).reshape(route_lists.shape)


def contract(left, right, left_dim, right_dim):
    return lax.dot_general(
        left, right, (((left_dim,), (right_dim,)), ((), ())), preferred_element_type=jnp.float32
    )


def expert_work(token_rows, cot_rows, w_gate, w_up, w_down):
    pre_gate = contract(token_rows, w_gate, 1, 1)
    pre_up = contract(token_rows, w_up, 1, 1)
    sigmoid_gate = jax.nn.sigmoid(pre_gate)
    activated = pre_gate * sigmoid_gate
    hidden = (activated * pre_up).astype(jnp.bfloat16)
    grad_hidden = contract(cot_rows, w_down, 1, 1)
    grad_gate = (
        grad_hidden * pre_up * sigmoid_gate * (1.0 + pre_gate * (1.0 - sigmoid_gate))
    ).astype(jnp.bfloat16)
    grad_up = (grad_hidden * activated).astype(jnp.bfloat16)
    gate_grad = contract(grad_gate, token_rows, 0, 0)
    up_grad = contract(grad_up, token_rows, 0, 0)
    down_grad = contract(hidden, cot_rows, 0, 0)
    row_grads = (
        jnp.dot(grad_gate, w_gate, preferred_element_type=jnp.float32)
        + jnp.dot(grad_up, w_up, preferred_element_type=jnp.float32)
    ).astype(jnp.bfloat16)
    return (row_grads, gate_grad, up_grad, down_grad)


def on_device(
    tokens,
    cotangent,
    routes,
    gates,
    plan,
    gate_values,
    up_values,
    down_values,
    gate_scales,
    up_scales,
    down_scales,
):
    tok_count, features = tokens.shape
    n_x, n_z, n_c = (lax.axis_size(a) for a in EXPERT_AXES)
    ring = n_z * n_c
    experts = n_x * ring
    replicas = lax.axis_size("dp")
    capacity = 2
    half_bit = experts.bit_length() - 2
    ring_index = lax.axis_index("ez") * n_c + lax.axis_index("ec")
    expert_index = lax.axis_index("ex") * ring + ring_index
    numbers = jnp.arange(experts, dtype=jnp.int32)
    is_moved = jnp.sum(jnp.where(numbers == expert_index, plan, 0)) != expert_index
    own = (
        jnp.concatenate([gate_values, up_values, down_values], axis=0),
        jnp.concatenate([gate_scales, up_scales, down_scales], axis=0),
    )
    partner = swapped(own, EXPERT_AXES, experts, half_bit)
    values, scales = (jnp.where(is_moved, b, a) for a, b in zip(own, partner))
    w_gate, w_up, w_down = (dequantize(values[i], scales[i]) for i in range(3))

    destination = jnp.take(plan, routes, axis=0)
    position = slot_position(destination, experts, capacity)
    slots = jnp.arange(experts * capacity, dtype=jnp.int32)
    dispatch = jnp.any(position[..., None] == slots, axis=1).astype(jnp.bfloat16).reshape(
        tok_count, experts, capacity
    )
    pad = jnp.zeros((tok_count, 128 - 2 * position.shape[1]), jnp.bfloat16)
    packed = jnp.concatenate(
        [tokens, cotangent, position.astype(jnp.bfloat16), gates, pad], axis=1
    )
    ring_rows = lax.all_gather(packed, "ez", axis=0, tiled=True)
    top = position.shape[1]
    ring_position = ring_rows[:, 2 * features:2 * features + top].astype(jnp.int32)
    ring_gates = ring_rows[:, 2 * features + top:2 * features + 2 * top]
    my_z = lax.axis_index("ez")
    target = (
        ((jnp.arange(n_x, dtype=jnp.int32)[:, None, None] * n_z + my_z) * n_c
         + jnp.arange(n_c, dtype=jnp.int32)[None, :, None]) * capacity
        + jnp.arange(capacity, dtype=jnp.int32)
    )
    match = ring_position[:, :, None, None, None] == target
    picked = jnp.any(match, axis=1).astype(jnp.bfloat16).reshape(n_z, tok_count, n_x, n_c, capacity)
    picked_gate = jnp.sum(
        jnp.where(match, ring_gates[:, :, None, None, None], jnp.zeros((), ring_gates.dtype)), axis=1
    ).reshape(n_z, tok_count, n_x, n_c, capacity)
    ring_rows = ring_rows.reshape(n_z, tok_count, ring_rows.shape[-1])
    relay_tok = jnp.einsum(
        "zrxcs,zrd->sxczd", picked, ring_rows[:, :, :features], preferred_element_type=jnp.float32
    ).astype(jnp.bfloat16).reshape(capacity, n_x * n_c, n_z, features)
    relay_cot = jnp.einsum(
        "zrxcs,zrd->sxczd", picked_gate, ring_rows[:, :, features:2 * features],
        preferred_element_type=jnp.float32,
    ).astype(jnp.bfloat16).reshape(capacity, n_x * n_c, n_z, features)
    dispatch = dispatch.reshape(tok_count, n_x, n_z, n_c, capacity).transpose(0, 1, 3, 2, 4).reshape(
        tok_count, experts, capacity
    )

    token_sum = jnp.zeros((tok_count, features), jnp.float32)
    sums = None
    for chunk in range(capacity):
        both = jnp.stack([relay_tok[chunk], relay_cot[chunk]], axis=0)
        arrived = lax.all_to_all(both, ("ex", "ec"), split_axis=1, concat_axis=1, tiled=True)
        arrived = arrived.reshape(2, experts, features)
        gathered = lax.all_gather(arrived, "dp", axis=1, tiled=True)
        row_grads, gate_grad, up_grad, down_grad = expert_work(
            gathered[0], gathered[1], w_gate, w_up, w_down
        )
        part = (gate_grad, up_grad, down_grad)
        sums = part if sums is None else tuple(a + b for a, b in zip(sums, part))
        summed_rows = lax.psum_scatter(
            row_grads.reshape(replicas, experts, features), "dp", scatter_dimension=0, tiled=True
        )
        returned = lax.all_to_all(
            summed_rows[0], ("ex", "ec", "ez"), split_axis=0, concat_axis=0, tiled=True
        )
        token_sum = token_sum + jnp.einsum(
            "re,ed->rd", dispatch[:, :, chunk], returned, preferred_element_type=jnp.float32
        )
    token_grads = token_sum.astype(jnp.bfloat16)
    gate_grad, up_grad, down_grad = (x.astype(jnp.bfloat16) for x in sums)
    return (token_grads, gate_grad[None], up_grad[None], down_grad[None])


def split_mesh(mesh):
    devices = mesh.devices
    flat = devices.reshape(-1)
    sizes = []
    for pick in (lambda d: d.coords[0], lambda d: d.coords[2], lambda d: d.core_on_chip):
        sizes.append(len({pick(d) for d in devices[0]}))
    assert int(np.prod(sizes)) == devices.shape[1]
    return Mesh(flat.reshape((devices.shape[0], *sizes)), ("dp", *EXPERT_AXES))


def solution(mesh):
    fine = split_mesh(mesh)
    rows = P(("dp", *EXPERT_AXES), None)
    weights = P(EXPERT_AXES, "dp", None)
    return jax.shard_map(
        on_device,
        mesh=fine,
        in_specs=(rows, rows, rows, rows, P(), weights, weights, weights, weights, weights, weights),
        out_specs=(rows, weights, weights, weights),
        check_vma=False,
    )
```

```python
import jax
import jax.numpy as jnp
import numpy as np
from jax import lax
from jax.sharding import Mesh
from jax.sharding import PartitionSpec as P

EXPERT_AXES = ("ex", "ez", "ec")


def swapped(block, axis, count, stride):
    route = []
    for low in range(count):
        high = low | 1 << stride
        if high != low and high < count:
            route += [(low, high), (high, low)]
    return lax.ppermute(block, axis, route)


def dequantize(values, scales):
    row_block = values.shape[0] // scales.shape[0]
    col_block = values.shape[1] // scales.shape[1]
    spread = jnp.repeat(jnp.repeat(scales, row_block, axis=0), col_block, axis=1)
    return (values.astype(jnp.float32) * spread).astype(jnp.bfloat16)


def slot_position(route_lists, experts, capacity):
    numbers = jnp.arange(experts, dtype=jnp.int32)
    flattened = route_lists.reshape(-1)
    marked = (flattened[:, None] == numbers).astype(jnp.int32)
    slot_index = jnp.sum((jnp.cumsum(marked, axis=0) - 1) * marked, axis=-1)
    return (flattened * capacity + slot_index).reshape(route_lists.shape)


def dp_gather(block, count):
    shifted = [lax.ppermute(block, "dp", [(i, (i + r) % count) for i in range(count)]) for r in range(1, count)]
    return [block] + shifted


def dp_reduce(parts, count):
    total = parts[0].astype(jnp.float32)
    for r in range(1, count):
        total = total + lax.ppermute(
            parts[r], "dp", [(i, (i - r) % count) for i in range(count)]
        ).astype(jnp.float32)
    return total


def contract(left, right, left_dim, right_dim):
    return lax.dot_general(
        left, right, (((left_dim,), (right_dim,)), ((), ())), preferred_element_type=jnp.float32
    )


def expert_work(token_rows, cot_rows, w_gate, w_up, w_down):
    pre_gate = contract(token_rows, w_gate, 1, 1)
    pre_up = contract(token_rows, w_up, 1, 1)
    sigmoid_gate = jax.nn.sigmoid(pre_gate)
    activated = pre_gate * sigmoid_gate
    hidden = (activated * pre_up).astype(jnp.bfloat16)
    grad_hidden = contract(cot_rows, w_down, 1, 1)
    grad_gate = (
        grad_hidden * pre_up * sigmoid_gate * (1.0 + pre_gate * (1.0 - sigmoid_gate))
    ).astype(jnp.bfloat16)
    grad_up = (grad_hidden * activated).astype(jnp.bfloat16)
    gate_grad = contract(grad_gate, token_rows, 0, 0)
    up_grad = contract(grad_up, token_rows, 0, 0)
    down_grad = contract(hidden, cot_rows, 0, 0)
    row_grads = (
        jnp.dot(grad_gate, w_gate, preferred_element_type=jnp.float32)
        + jnp.dot(grad_up, w_up, preferred_element_type=jnp.float32)
    ).astype(jnp.bfloat16)
    return (row_grads, gate_grad, up_grad, down_grad)


def on_device(
    tokens,
    cotangent,
    routes,
    gates,
    plan,
    gate_values,
    up_values,
    down_values,
    gate_scales,
    up_scales,
    down_scales,
):
    tok_count, features = tokens.shape
    n_x, n_z, n_c = (lax.axis_size(a) for a in EXPERT_AXES)
    ring = n_z * n_c
    experts = n_x * ring
    replicas = lax.axis_size("dp")
    capacity = 2
    half_bit = experts.bit_length() - 2
    ring_index = lax.axis_index("ez") * n_c + lax.axis_index("ec")
    expert_index = lax.axis_index("ex") * ring + ring_index
    numbers = jnp.arange(experts, dtype=jnp.int32)
    is_moved = jnp.sum(jnp.where(numbers == expert_index, plan, 0)) != expert_index
    own = (
        jnp.concatenate([gate_values, up_values, down_values], axis=0),
        jnp.concatenate([gate_scales, up_scales, down_scales], axis=0),
    )
    partner = swapped(own, EXPERT_AXES, experts, half_bit)
    values, scales = (jnp.where(is_moved, b, a) for a, b in zip(own, partner))
    w_gate, w_up, w_down = (dequantize(values[i], scales[i]) for i in range(3))

    destination = jnp.take(plan, routes, axis=0)
    position = slot_position(destination, experts, capacity)
    slots = jnp.arange(experts * capacity, dtype=jnp.int32)
    dispatch = jnp.any(position[..., None] == slots, axis=1).astype(jnp.bfloat16).reshape(
        tok_count, experts, capacity
    )
    pad = jnp.zeros((tok_count, 128 - 2 * position.shape[1]), jnp.bfloat16)
    packed = jnp.concatenate(
        [tokens, cotangent, position.astype(jnp.bfloat16), gates, pad], axis=1
    )
    ring_rows = lax.all_gather(packed, "ez", axis=0, tiled=True)
    top = position.shape[1]
    ring_position = ring_rows[:, 2 * features:2 * features + top].astype(jnp.int32)
    ring_gates = ring_rows[:, 2 * features + top:2 * features + 2 * top]
    my_z = lax.axis_index("ez")
    target = (
        ((jnp.arange(n_x, dtype=jnp.int32)[:, None, None] * n_z + my_z) * n_c
         + jnp.arange(n_c, dtype=jnp.int32)[None, :, None]) * capacity
        + jnp.arange(capacity, dtype=jnp.int32)
    )
    match = ring_position[:, :, None, None, None] == target
    picked = jnp.any(match, axis=1).astype(jnp.bfloat16).reshape(n_z, tok_count, n_x, n_c, capacity)
    picked_gate = jnp.sum(
        jnp.where(match, ring_gates[:, :, None, None, None], jnp.zeros((), ring_gates.dtype)), axis=1
    ).reshape(n_z, tok_count, n_x, n_c, capacity)
    ring_rows = ring_rows.reshape(n_z, tok_count, ring_rows.shape[-1])
    relay_tok = jnp.einsum(
        "zrxcs,zrd->sxczd", picked, ring_rows[:, :, :features], preferred_element_type=jnp.float32
    ).astype(jnp.bfloat16).reshape(capacity, n_x * n_c, n_z, features)
    relay_cot = jnp.einsum(
        "zrxcs,zrd->sxczd", picked_gate, ring_rows[:, :, features:2 * features],
        preferred_element_type=jnp.float32,
    ).astype(jnp.bfloat16).reshape(capacity, n_x * n_c, n_z, features)
    dispatch = dispatch.reshape(tok_count, n_x, n_z, n_c, capacity).transpose(0, 1, 3, 2, 4).reshape(
        tok_count, experts, capacity
    )

    token_sum = jnp.zeros((tok_count, features), jnp.float32)
    sums = None
    for chunk in range(capacity):
        both = jnp.stack([relay_tok[chunk], relay_cot[chunk]], axis=0)
        arrived = lax.all_to_all(both, ("ex", "ec"), split_axis=1, concat_axis=1, tiled=True)
        arrived = arrived.reshape(2, experts, features)
        blocks = dp_gather(arrived, replicas)
        token_rows = jnp.concatenate([b[0] for b in blocks], axis=0)
        cot_rows = jnp.concatenate([b[1] for b in blocks], axis=0)
        row_grads, gate_grad, up_grad, down_grad = expert_work(
            token_rows, cot_rows, w_gate, w_up, w_down
        )
        part = (gate_grad, up_grad, down_grad)
        sums = part if sums is None else tuple(a + b for a, b in zip(sums, part))
        summed_rows = dp_reduce(row_grads.reshape(replicas, experts, features), replicas)
        returned = lax.all_to_all(
            summed_rows.astype(jnp.bfloat16), ("ex", "ec", "ez"), split_axis=0, concat_axis=0, tiled=True
        )
        token_sum = token_sum + jnp.einsum(
            "re,ed->rd", dispatch[:, :, chunk], returned, preferred_element_type=jnp.float32
        )
    token_grads = token_sum.astype(jnp.bfloat16)
    gate_grad, up_grad, down_grad = (x.astype(jnp.bfloat16) for x in sums)
    return (token_grads, gate_grad[None], up_grad[None], down_grad[None])


def split_mesh(mesh):
    devices = mesh.devices
    flat = devices.reshape(-1)
    sizes = []
    for pick in (lambda d: d.coords[0], lambda d: d.coords[2], lambda d: d.core_on_chip):
        sizes.append(len({pick(d) for d in devices[0]}))
    assert int(np.prod(sizes)) == devices.shape[1]
    return Mesh(flat.reshape((devices.shape[0], *sizes)), ("dp", *EXPERT_AXES))


def solution(mesh):
    fine = split_mesh(mesh)
    rows = P(("dp", *EXPERT_AXES), None)
    weights = P(EXPERT_AXES, "dp", None)
    return jax.shard_map(
        on_device,
        mesh=fine,
        in_specs=(rows, rows, rows, rows, P(), weights, weights, weights, weights, weights, weights),
        out_specs=(rows, weights, weights, weights),
        check_vma=False,
    )
```

```python
import jax
import jax.numpy as jnp
from jax import lax
from jax.sharding import PartitionSpec as P


def swapped(block, axis, stride):
    count = lax.axis_size(axis)
    route = []
    for low in range(count):
        high = low | 1 << stride
        if high != low and high < count:
            route += [(low, high), (high, low)]
    return lax.ppermute(block, axis, route)


def dequantize(values, scales):
    row_block = values.shape[0] // scales.shape[0]
    col_block = values.shape[1] // scales.shape[1]
    spread = jnp.repeat(jnp.repeat(scales, row_block, axis=0), col_block, axis=1)
    return (values.astype(jnp.float32) * spread).astype(jnp.bfloat16)


def slot_choice(route_lists, experts, capacity):
    numbers = jnp.arange(experts, dtype=jnp.int32)
    flattened = route_lists.reshape(-1)
    marked = (flattened[:, None] == numbers).astype(jnp.int32)
    slot_index = jnp.sum((jnp.cumsum(marked, axis=0) - 1) * marked, axis=-1)
    position = flattened * capacity + slot_index
    selected = position[:, None] == jnp.arange(experts * capacity, dtype=jnp.int32)
    return selected.reshape(route_lists.shape + (experts * capacity,))


def contract(left, right, left_dim, right_dim):
    return lax.dot_general(
        left, right, (((left_dim,), (right_dim,)), ((), ())), preferred_element_type=jnp.float32
    )


def expert_work(token_rows, cot_rows, w_gate, w_up, w_down):
    pre_gate = contract(token_rows, w_gate, 1, 1)
    pre_up = contract(token_rows, w_up, 1, 1)
    sigmoid_gate = jax.nn.sigmoid(pre_gate)
    activated = pre_gate * sigmoid_gate
    hidden = (activated * pre_up).astype(jnp.bfloat16)
    grad_hidden = contract(cot_rows, w_down, 1, 1)
    grad_gate = (
        grad_hidden * pre_up * sigmoid_gate * (1.0 + pre_gate * (1.0 - sigmoid_gate))
    ).astype(jnp.bfloat16)
    grad_up = (grad_hidden * activated).astype(jnp.bfloat16)
    gate_grad = contract(grad_gate, token_rows, 0, 0)
    up_grad = contract(grad_up, token_rows, 0, 0)
    down_grad = contract(hidden, cot_rows, 0, 0)
    row_grads = (
        jnp.dot(grad_gate, w_gate, preferred_element_type=jnp.float32)
        + jnp.dot(grad_up, w_up, preferred_element_type=jnp.float32)
    ).astype(jnp.bfloat16)
    return (row_grads, gate_grad, up_grad, down_grad)


def on_device(
    tokens,
    cotangent,
    routes,
    gates,
    plan,
    gate_values,
    up_values,
    down_values,
    gate_scales,
    up_scales,
    down_scales,
):
    tok_count, features = tokens.shape
    experts = lax.axis_size("expert")
    replicas = lax.axis_size("dp")
    capacity = 2
    half_bit = experts.bit_length() - 2
    expert_index = lax.axis_index("expert")
    numbers = jnp.arange(experts, dtype=jnp.int32)
    is_moved = jnp.sum(jnp.where(numbers == expert_index, plan, 0)) != expert_index
    own = (
        jnp.concatenate([gate_values, up_values, down_values], axis=0),
        jnp.concatenate([gate_scales, up_scales, down_scales], axis=0),
    )
    partner = swapped(own, "expert", half_bit)
    values, scales = (jnp.where(is_moved, b, a) for a, b in zip(own, partner))
    w_gate, w_up, w_down = (dequantize(values[i], scales[i]) for i in range(3))
    destination = jnp.take(plan, routes, axis=0)
    selected = slot_choice(destination, experts, capacity)
    dispatch = jnp.sum(selected.astype(jnp.int32), axis=1).reshape(
        tok_count, experts, capacity
    ).astype(jnp.bfloat16)
    outgoing = jnp.einsum(
        "rec,rd->ecd", dispatch, tokens, preferred_element_type=jnp.float32
    ).astype(jnp.bfloat16)
    slot_gate = jnp.einsum(
        "rkx,rk->x", selected.astype(jnp.float32), gates.astype(jnp.float32)
    ).reshape(experts, capacity)
    lifted = jnp.einsum("rec,rd->ecd", dispatch, cotangent, preferred_element_type=jnp.float32)
    cot_out = (lifted * slot_gate[..., None]).astype(jnp.bfloat16)
    token_sum = jnp.zeros((tok_count, features), jnp.float32)
    sums = None
    for chunk in range(capacity):
        both = jnp.stack([outgoing[:, chunk], cot_out[:, chunk]], axis=0)
        arrived = lax.all_to_all(both, "expert", split_axis=1, concat_axis=1, tiled=True)
        if chunk == 0:
            gathered = lax.all_gather(arrived, "dp", axis=1, tiled=True)
        else:
            spread = jnp.broadcast_to(arrived[None], (replicas,) + arrived.shape)
            gathered = lax.all_to_all(spread, "dp", split_axis=0, concat_axis=0, tiled=True)
            gathered = jnp.moveaxis(gathered, 0, 1).reshape(2, replicas * experts, features)
        row_grads, gate_grad, up_grad, down_grad = expert_work(
            gathered[0], gathered[1], w_gate, w_up, w_down
        )
        part = (gate_grad, up_grad, down_grad)
        sums = part if sums is None else tuple(a + b for a, b in zip(sums, part))
        summed_rows = lax.psum_scatter(
            row_grads.reshape(replicas, experts, features), "dp", scatter_dimension=0, tiled=True
        )
        returned = lax.all_to_all(summed_rows[0], "expert", split_axis=0, concat_axis=0, tiled=True)
        token_sum = token_sum + jnp.einsum(
            "re,ed->rd", dispatch[:, :, chunk], returned, preferred_element_type=jnp.float32
        )
    token_grads = token_sum.astype(jnp.bfloat16)
    gate_grad, up_grad, down_grad = (x.astype(jnp.bfloat16) for x in sums)
    return (token_grads, gate_grad[None], up_grad[None], down_grad[None])


def solution(mesh):
    return jax.shard_map(
        on_device,
        mesh=mesh,
        in_specs=(
            P(("dp", "expert"), None),
            P(("dp", "expert"), None),
            P(("dp", "expert"), None),
            P(("dp", "expert"), None),
            P(),
            P("expert", "dp", None),
            P("expert", "dp", None),
            P("expert", "dp", None),
            P("expert", "dp", None),
            P("expert", "dp", None),
            P("expert", "dp", None),
        ),
        out_specs=(
            P(("dp", "expert"), None),
            P("expert", "dp", None),
            P("expert", "dp", None),
            P("expert", "dp", None),
        ),
        check_vma=False,
    )
```

```python
import jax
import jax.numpy as jnp
from jax import lax
from jax.sharding import PartitionSpec as P


def swapped(block, axis, stride):
    count = lax.axis_size(axis)
    route = []
    for low in range(count):
        high = low | 1 << stride
        if high != low and high < count:
            route += [(low, high), (high, low)]
    return lax.ppermute(block, axis, route)


def dequantize(values, scales):
    row_block = values.shape[0] // scales.shape[0]
    col_block = values.shape[1] // scales.shape[1]
    spread = jnp.repeat(jnp.repeat(scales, row_block, axis=0), col_block, axis=1)
    return (values.astype(jnp.float32) * spread).astype(jnp.bfloat16)


def slot_choice(route_lists, experts, capacity):
    numbers = jnp.arange(experts, dtype=jnp.int32)
    flattened = route_lists.reshape(-1)
    marked = (flattened[:, None] == numbers).astype(jnp.int32)
    slot_index = jnp.sum((jnp.cumsum(marked, axis=0) - 1) * marked, axis=-1)
    position = flattened * capacity + slot_index
    selected = position[:, None] == jnp.arange(experts * capacity, dtype=jnp.int32)
    return selected.reshape(route_lists.shape + (experts * capacity,))


def contract(left, right, left_dim, right_dim):
    return lax.dot_general(
        left, right, (((left_dim,), (right_dim,)), ((), ())), preferred_element_type=jnp.float32
    )


def expert_work(token_rows, cot_rows, w_gate, w_up, w_down):
    pre_gate = contract(token_rows, w_gate, 1, 1)
    pre_up = contract(token_rows, w_up, 1, 1)
    sigmoid_gate = jax.nn.sigmoid(pre_gate)
    activated = pre_gate * sigmoid_gate
    hidden = (activated * pre_up).astype(jnp.bfloat16)
    grad_hidden = contract(cot_rows, w_down, 1, 1)
    grad_gate = (
        grad_hidden * pre_up * sigmoid_gate * (1.0 + pre_gate * (1.0 - sigmoid_gate))
    ).astype(jnp.bfloat16)
    grad_up = (grad_hidden * activated).astype(jnp.bfloat16)
    gate_grad = contract(grad_gate, token_rows, 0, 0)
    up_grad = contract(grad_up, token_rows, 0, 0)
    down_grad = contract(hidden, cot_rows, 0, 0)
    row_grads = (
        jnp.dot(grad_gate, w_gate, preferred_element_type=jnp.float32)
        + jnp.dot(grad_up, w_up, preferred_element_type=jnp.float32)
    ).astype(jnp.bfloat16)
    return (row_grads, gate_grad, up_grad, down_grad)


def on_device(
    tokens,
    cotangent,
    routes,
    gates,
    plan,
    gate_values,
    up_values,
    down_values,
    gate_scales,
    up_scales,
    down_scales,
):
    tok_count, features = tokens.shape
    experts = lax.axis_size("expert")
    replicas = lax.axis_size("dp")
    capacity = 2
    half_bit = experts.bit_length() - 2
    expert_index = lax.axis_index("expert")
    numbers = jnp.arange(experts, dtype=jnp.int32)
    is_moved = jnp.sum(jnp.where(numbers == expert_index, plan, 0)) != expert_index
    own = (
        jnp.concatenate([gate_values, up_values, down_values], axis=0),
        jnp.concatenate([gate_scales, up_scales, down_scales], axis=0),
    )
    partner = swapped(own, "expert", half_bit)
    values, scales = (jnp.where(is_moved, b, a) for a, b in zip(own, partner))
    w_gate, w_up, w_down = (dequantize(values[i], scales[i]) for i in range(3))
    destination = jnp.take(plan, routes, axis=0)
    selected = slot_choice(destination, experts, capacity)
    dispatch = jnp.sum(selected.astype(jnp.int32), axis=1).reshape(
        tok_count, experts, capacity
    ).astype(jnp.bfloat16)
    outgoing = jnp.einsum(
        "rec,rd->ecd", dispatch, tokens, preferred_element_type=jnp.float32
    ).astype(jnp.bfloat16)
    slot_gate = jnp.einsum(
        "rkx,rk->x", selected.astype(jnp.float32), gates.astype(jnp.float32)
    ).reshape(experts, capacity)
    lifted = jnp.einsum("rec,rd->ecd", dispatch, cotangent, preferred_element_type=jnp.float32)
    cot_out = (lifted * slot_gate[..., None]).astype(jnp.bfloat16)
    token_sum = jnp.zeros((tok_count, features), jnp.float32)
    sums = None
    for chunk in range(capacity):
        both = jnp.stack([outgoing[:, chunk], cot_out[:, chunk]], axis=0)
        arrived = lax.all_to_all(both, "expert", split_axis=1, concat_axis=1, tiled=True)
        gathered = lax.all_gather(arrived, "dp", axis=1, tiled=True)
        row_grads, gate_grad, up_grad, down_grad = expert_work(
            gathered[0], gathered[1], w_gate, w_up, w_down
        )
        part = (gate_grad, up_grad, down_grad)
        sums = part if sums is None else tuple(a + b for a, b in zip(sums, part))
        pieces = lax.all_to_all(
            row_grads.reshape(replicas, experts, features), "dp", split_axis=0, concat_axis=0, tiled=True
        )
        summed_rows = jnp.sum(pieces.astype(jnp.float32), axis=0).astype(jnp.bfloat16)
        returned = lax.all_to_all(summed_rows, "expert", split_axis=0, concat_axis=0, tiled=True)
        token_sum = token_sum + jnp.einsum(
            "re,ed->rd", dispatch[:, :, chunk], returned, preferred_element_type=jnp.float32
        )
    token_grads = token_sum.astype(jnp.bfloat16)
    gate_grad, up_grad, down_grad = (x.astype(jnp.bfloat16) for x in sums)
    return (token_grads, gate_grad[None], up_grad[None], down_grad[None])


def solution(mesh):
    return jax.shard_map(
        on_device,
        mesh=mesh,
        in_specs=(
            P(("dp", "expert"), None),
            P(("dp", "expert"), None),
            P(("dp", "expert"), None),
            P(("dp", "expert"), None),
            P(),
            P("expert", "dp", None),
            P("expert", "dp", None),
            P("expert", "dp", None),
            P("expert", "dp", None),
            P("expert", "dp", None),
            P("expert", "dp", None),
        ),
        out_specs=(
            P(("dp", "expert"), None),
            P("expert", "dp", None),
            P("expert", "dp", None),
            P("expert", "dp", None),
        ),
        check_vma=False,
    )
```

```python
import jax
import jax.numpy as jnp
import numpy as np
from jax import lax
from jax.sharding import Mesh
from jax.sharding import PartitionSpec as P

EXPERT_AXES = ("ex", "ez", "ec")


def swapped(block, axis, count, stride):
    route = []
    for low in range(count):
        high = low | 1 << stride
        if high != low and high < count:
            route += [(low, high), (high, low)]
    return lax.ppermute(block, axis, route)


def dequantize(values, scales):
    row_block = values.shape[0] // scales.shape[0]
    col_block = values.shape[1] // scales.shape[1]
    spread = jnp.repeat(jnp.repeat(scales, row_block, axis=0), col_block, axis=1)
    return (values.astype(jnp.float32) * spread).astype(jnp.bfloat16)


def slot_position(route_lists, experts, capacity):
    numbers = jnp.arange(experts, dtype=jnp.int32)
    flattened = route_lists.reshape(-1)
    marked = (flattened[:, None] == numbers).astype(jnp.int32)
    slot_index = jnp.sum((jnp.cumsum(marked, axis=0) - 1) * marked, axis=-1)
    return (flattened * capacity + slot_index).reshape(route_lists.shape)


def contract(left, right, left_dim, right_dim):
    return lax.dot_general(
        left, right, (((left_dim,), (right_dim,)), ((), ())), preferred_element_type=jnp.float32
    )


def expert_work(token_rows, cot_rows, w_gate, w_up, w_down):
    pre_gate = contract(token_rows, w_gate, 1, 1)
    pre_up = contract(token_rows, w_up, 1, 1)
    sigmoid_gate = jax.nn.sigmoid(pre_gate)
    activated = pre_gate * sigmoid_gate
    hidden = (activated * pre_up).astype(jnp.bfloat16)
    grad_hidden = contract(cot_rows, w_down, 1, 1)
    grad_gate = (
        grad_hidden * pre_up * sigmoid_gate * (1.0 + pre_gate * (1.0 - sigmoid_gate))
    ).astype(jnp.bfloat16)
    grad_up = (grad_hidden * activated).astype(jnp.bfloat16)
    gate_grad = contract(grad_gate, token_rows, 0, 0)
    up_grad = contract(grad_up, token_rows, 0, 0)
    down_grad = contract(hidden, cot_rows, 0, 0)
    row_grads = (
        jnp.dot(grad_gate, w_gate, preferred_element_type=jnp.float32)
        + jnp.dot(grad_up, w_up, preferred_element_type=jnp.float32)
    ).astype(jnp.bfloat16)
    return (row_grads, gate_grad, up_grad, down_grad)


def on_device(
    tokens,
    cotangent,
    routes,
    gates,
    plan,
    gate_values,
    up_values,
    down_values,
    gate_scales,
    up_scales,
    down_scales,
):
    tok_count, features = tokens.shape
    n_x, n_z, n_c = (lax.axis_size(a) for a in EXPERT_AXES)
    ring = n_z * n_c
    experts = n_x * ring
    replicas = lax.axis_size("dp")
    capacity = 2
    half_bit = experts.bit_length() - 2
    ring_index = lax.axis_index("ez") * n_c + lax.axis_index("ec")
    expert_index = lax.axis_index("ex") * ring + ring_index
    numbers = jnp.arange(experts, dtype=jnp.int32)
    is_moved = jnp.sum(jnp.where(numbers == expert_index, plan, 0)) != expert_index
    own = (
        jnp.concatenate([gate_values, up_values, down_values], axis=0),
        jnp.concatenate([gate_scales, up_scales, down_scales], axis=0),
    )
    partner = swapped(own, EXPERT_AXES, experts, half_bit)
    values, scales = (jnp.where(is_moved, b, a) for a, b in zip(own, partner))
    w_gate, w_up, w_down = (dequantize(values[i], scales[i]) for i in range(3))

    destination = jnp.take(plan, routes, axis=0)
    position = slot_position(destination, experts, capacity)
    slots = jnp.arange(experts * capacity, dtype=jnp.int32)
    dispatch = jnp.any(position[..., None] == slots, axis=1).astype(jnp.bfloat16).reshape(
        tok_count, experts, capacity
    )
    gate_pick = jnp.sum(
        jnp.where(position[..., None] == slots, gates[..., None], jnp.zeros((), gates.dtype)), axis=1
    ).reshape(tok_count, experts, capacity)
    first_tok = jnp.einsum(
        "re,rd->ed", dispatch[:, :, 0], tokens, preferred_element_type=jnp.float32
    ).astype(jnp.bfloat16)
    first_cot = jnp.einsum(
        "re,rd->ed", gate_pick[:, :, 0], cotangent, preferred_element_type=jnp.float32
    ).astype(jnp.bfloat16)
    pad = jnp.zeros((tok_count, 128 - 2 * position.shape[1]), jnp.bfloat16)
    packed = jnp.concatenate(
        [tokens, cotangent, position.astype(jnp.bfloat16), gates, pad], axis=1
    )
    ring_rows = lax.all_gather(packed, "ez", axis=0, tiled=True)
    top = position.shape[1]
    ring_position = ring_rows[:, 2 * features:2 * features + top].astype(jnp.int32)
    ring_gates = ring_rows[:, 2 * features + top:2 * features + 2 * top]
    my_z = lax.axis_index("ez")
    target = (
        (jnp.arange(n_x, dtype=jnp.int32)[:, None] * n_z + my_z) * n_c
        + jnp.arange(n_c, dtype=jnp.int32)
    ) * capacity + 1
    match = ring_position[:, :, None, None] == target
    picked = jnp.any(match, axis=1).astype(jnp.bfloat16).reshape(n_z, tok_count, n_x, n_c)
    picked_gate = jnp.sum(
        jnp.where(match, ring_gates[:, :, None, None], jnp.zeros((), ring_gates.dtype)), axis=1
    ).reshape(n_z, tok_count, n_x, n_c)
    ring_rows = ring_rows.reshape(n_z, tok_count, ring_rows.shape[-1])
    relay_tok = jnp.einsum(
        "zrxc,zrd->xczd", picked, ring_rows[:, :, :features], preferred_element_type=jnp.float32
    ).astype(jnp.bfloat16).reshape(n_x * n_c, n_z, features)
    relay_cot = jnp.einsum(
        "zrxc,zrd->xczd", picked_gate, ring_rows[:, :, features:2 * features],
        preferred_element_type=jnp.float32,
    ).astype(jnp.bfloat16).reshape(n_x * n_c, n_z, features)
    relay_tok, relay_cot, w_gate, w_up, w_down = lax.optimization_barrier(
        (relay_tok, relay_cot, w_gate, w_up, w_down)
    )
    dispatch_relay = dispatch[:, :, 1].reshape(tok_count, n_x, n_z, n_c).transpose(0, 1, 3, 2).reshape(
        tok_count, experts
    )

    token_sum = jnp.zeros((tok_count, features), jnp.float32)
    sums = None
    for chunk in range(capacity):
        if chunk == 0:
            both = jnp.stack([first_tok, first_cot], axis=0)
            arrived = lax.all_to_all(both, EXPERT_AXES, split_axis=1, concat_axis=1, tiled=True)
            back_axes, back_dispatch = EXPERT_AXES, dispatch[:, :, 0]
        else:
            both = jnp.stack([relay_tok, relay_cot], axis=0)
            arrived = lax.all_to_all(both, ("ex", "ec"), split_axis=1, concat_axis=1, tiled=True)
            back_axes, back_dispatch = ("ex", "ec", "ez"), dispatch_relay
        arrived = arrived.reshape(2, experts, features)
        gathered = lax.all_gather(arrived, "dp", axis=1, tiled=True)
        row_grads, gate_grad, up_grad, down_grad = expert_work(
            gathered[0], gathered[1], w_gate, w_up, w_down
        )
        part = (gate_grad, up_grad, down_grad)
        sums = part if sums is None else tuple(a + b for a, b in zip(sums, part))
        summed_rows = lax.psum_scatter(
            row_grads.reshape(replicas, experts, features), "dp", scatter_dimension=0, tiled=True
        )
        returned = lax.all_to_all(summed_rows[0], back_axes, split_axis=0, concat_axis=0, tiled=True)
        token_sum = token_sum + jnp.einsum(
            "re,ed->rd", back_dispatch, returned, preferred_element_type=jnp.float32
        )
    token_grads = token_sum.astype(jnp.bfloat16)
    gate_grad, up_grad, down_grad = (x.astype(jnp.bfloat16) for x in sums)
    return (token_grads, gate_grad[None], up_grad[None], down_grad[None])


def split_mesh(mesh):
    devices = mesh.devices
    flat = devices.reshape(-1)
    sizes = []
    for pick in (lambda d: d.coords[0], lambda d: d.coords[2], lambda d: d.core_on_chip):
        sizes.append(len({pick(d) for d in devices[0]}))
    assert int(np.prod(sizes)) == devices.shape[1]
    return Mesh(flat.reshape((devices.shape[0], *sizes)), ("dp", *EXPERT_AXES))


def solution(mesh):
    fine = split_mesh(mesh)
    rows = P(("dp", *EXPERT_AXES), None)
    weights = P(EXPERT_AXES, "dp", None)
    return jax.shard_map(
        on_device,
        mesh=fine,
        in_specs=(rows, rows, rows, rows, P(), weights, weights, weights, weights, weights, weights),
        out_specs=(rows, weights, weights, weights),
        check_vma=False,
    )
```

```python
import jax
import jax.numpy as jnp
from jax import lax
from jax.sharding import PartitionSpec as P


def swapped(block, axis, stride):
    count = lax.axis_size(axis)
    route = []
    for low in range(count):
        high = low | 1 << stride
        if high != low and high < count:
            route += [(low, high), (high, low)]
    return lax.ppermute(block, axis, route)


def dequantize(values, scales):
    row_block = values.shape[0] // scales.shape[0]
    col_block = values.shape[1] // scales.shape[1]
    spread = jnp.repeat(jnp.repeat(scales, row_block, axis=0), col_block, axis=1)
    return (values.astype(jnp.float32) * spread).astype(jnp.bfloat16)


def slot_choice(route_lists, experts, capacity):
    numbers = jnp.arange(experts, dtype=jnp.int32)
    flattened = route_lists.reshape(-1)
    marked = (flattened[:, None] == numbers).astype(jnp.int32)
    slot_index = jnp.sum((jnp.cumsum(marked, axis=0) - 1) * marked, axis=-1)
    position = flattened * capacity + slot_index
    selected = position[:, None] == jnp.arange(experts * capacity, dtype=jnp.int32)
    return selected.reshape(route_lists.shape + (experts * capacity,))


def contract(left, right, left_dim, right_dim):
    return lax.dot_general(
        left, right, (((left_dim,), (right_dim,)), ((), ())), preferred_element_type=jnp.float32
    )


def expert_work(token_rows, cot_rows, w_gate, w_up, w_down):
    pre_gate = contract(token_rows, w_gate, 1, 1)
    pre_up = contract(token_rows, w_up, 1, 1)
    sigmoid_gate = jax.nn.sigmoid(pre_gate)
    activated = pre_gate * sigmoid_gate
    hidden = (activated * pre_up).astype(jnp.bfloat16)
    grad_hidden = contract(cot_rows, w_down, 1, 1)
    grad_gate = (
        grad_hidden * pre_up * sigmoid_gate * (1.0 + pre_gate * (1.0 - sigmoid_gate))
    ).astype(jnp.bfloat16)
    grad_up = (grad_hidden * activated).astype(jnp.bfloat16)
    gate_grad = contract(grad_gate, token_rows, 0, 0)
    up_grad = contract(grad_up, token_rows, 0, 0)
    down_grad = contract(hidden, cot_rows, 0, 0)
    row_grads = (
        jnp.dot(grad_gate, w_gate, preferred_element_type=jnp.float32)
        + jnp.dot(grad_up, w_up, preferred_element_type=jnp.float32)
    ).astype(jnp.bfloat16)
    return (row_grads, gate_grad, up_grad, down_grad)


def on_device(
    tokens,
    cotangent,
    routes,
    gates,
    plan,
    gate_values,
    up_values,
    down_values,
    gate_scales,
    up_scales,
    down_scales,
):
    tok_count, features = tokens.shape
    experts = lax.axis_size("expert")
    replicas = lax.axis_size("dp")
    capacity = 2
    half_bit = experts.bit_length() - 2
    expert_index = lax.axis_index("expert")
    numbers = jnp.arange(experts, dtype=jnp.int32)
    is_moved = jnp.sum(jnp.where(numbers == expert_index, plan, 0)) != expert_index
    own = (
        jnp.concatenate([gate_values, up_values, down_values], axis=0),
        jnp.concatenate([gate_scales, up_scales, down_scales], axis=0),
    )
    partner = swapped(own, "expert", half_bit)
    values, scales = (jnp.where(is_moved, b, a) for a, b in zip(own, partner))
    w_gate, w_up, w_down = (dequantize(values[i], scales[i]) for i in range(3))
    destination = jnp.take(plan, routes, axis=0)
    selected = slot_choice(destination, experts, capacity)
    dispatch = jnp.sum(selected.astype(jnp.int32), axis=1).reshape(
        tok_count, experts, capacity
    ).astype(jnp.bfloat16)
    slot_gate = jnp.einsum(
        "rkx,rk->rx", selected.astype(jnp.float32), gates.astype(jnp.float32)
    ).reshape(tok_count, experts, capacity).astype(jnp.bfloat16)
    zero = jnp.zeros_like(dispatch)
    pick = jnp.stack(
        [jnp.concatenate([dispatch, zero], axis=0), jnp.concatenate([zero, slot_gate], axis=0)], axis=0
    )
    sends = jnp.einsum(
        "srec,rd->csed", pick, jnp.concatenate([tokens, cotangent], axis=0),
        preferred_element_type=jnp.float32,
    ).astype(jnp.bfloat16)
    token_sum = jnp.zeros((tok_count, features), jnp.float32)
    sums = None
    for chunk in range(capacity):
        both = sends[chunk]
        arrived = lax.all_to_all(both, "expert", split_axis=1, concat_axis=1, tiled=True)
        gathered = lax.all_gather(arrived, "dp", axis=1, tiled=True)
        row_grads, gate_grad, up_grad, down_grad = expert_work(
            gathered[0], gathered[1], w_gate, w_up, w_down
        )
        part = (gate_grad, up_grad, down_grad)
        sums = part if sums is None else tuple(a + b for a, b in zip(sums, part))
        summed_rows = lax.psum_scatter(
            row_grads.reshape(replicas, experts, features), "dp", scatter_dimension=0, tiled=True
        )
        returned = lax.all_to_all(summed_rows[0], "expert", split_axis=0, concat_axis=0, tiled=True)
        token_sum = token_sum + jnp.einsum(
            "re,ed->rd", dispatch[:, :, chunk], returned, preferred_element_type=jnp.float32
        )
    token_grads = token_sum.astype(jnp.bfloat16)
    gate_grad, up_grad, down_grad = (x.astype(jnp.bfloat16) for x in sums)
    return (token_grads, gate_grad[None], up_grad[None], down_grad[None])


def solution(mesh):
    return jax.shard_map(
        on_device,
        mesh=mesh,
        in_specs=(
            P(("dp", "expert"), None),
            P(("dp", "expert"), None),
            P(("dp", "expert"), None),
            P(("dp", "expert"), None),
            P(),
            P("expert", "dp", None),
            P("expert", "dp", None),
            P("expert", "dp", None),
            P("expert", "dp", None),
            P("expert", "dp", None),
            P("expert", "dp", None),
        ),
        out_specs=(
            P(("dp", "expert"), None),
            P("expert", "dp", None),
            P("expert", "dp", None),
            P("expert", "dp", None),
        ),
        check_vma=False,
    )
```

```python
import jax
import jax.numpy as jnp
from jax import lax
from jax.sharding import PartitionSpec as P


def swapped(block, axis, stride):
    count = lax.axis_size(axis)
    route = []
    for low in range(count):
        high = low | 1 << stride
        if high != low and high < count:
            route += [(low, high), (high, low)]
    return lax.ppermute(block, axis, route)


def dequantize(values, scales):
    row_block = values.shape[0] // scales.shape[0]
    col_block = values.shape[1] // scales.shape[1]
    spread = jnp.repeat(jnp.repeat(scales, row_block, axis=0), col_block, axis=1)
    return (values.astype(jnp.float32) * spread).astype(jnp.bfloat16)


def slot_choice(route_lists, experts, capacity):
    numbers = jnp.arange(experts, dtype=jnp.int32)
    flattened = route_lists.reshape(-1)
    marked = (flattened[:, None] == numbers).astype(jnp.int32)
    slot_index = jnp.sum((jnp.cumsum(marked, axis=0) - 1) * marked, axis=-1)
    position = flattened * capacity + slot_index
    selected = position[:, None] == jnp.arange(experts * capacity, dtype=jnp.int32)
    return selected.reshape(route_lists.shape + (experts * capacity,))


def contract(left, right, left_dim, right_dim):
    return lax.dot_general(
        left, right, (((left_dim,), (right_dim,)), ((), ())), preferred_element_type=jnp.float32
    )


def expert_work(token_rows, cot_rows, w_gate, w_up, w_down):
    pre_gate = contract(token_rows, w_gate, 1, 1)
    pre_up = contract(token_rows, w_up, 1, 1)
    sigmoid_gate = jax.nn.sigmoid(pre_gate)
    activated = pre_gate * sigmoid_gate
    hidden = (activated * pre_up).astype(jnp.bfloat16)
    grad_hidden = contract(cot_rows, w_down, 1, 1)
    grad_gate = (
        grad_hidden * pre_up * sigmoid_gate * (1.0 + pre_gate * (1.0 - sigmoid_gate))
    ).astype(jnp.bfloat16)
    grad_up = (grad_hidden * activated).astype(jnp.bfloat16)
    gate_grad = contract(grad_gate, token_rows, 0, 0)
    up_grad = contract(grad_up, token_rows, 0, 0)
    down_grad = contract(hidden, cot_rows, 0, 0)
    row_grads = (
        jnp.dot(grad_gate, w_gate, preferred_element_type=jnp.float32)
        + jnp.dot(grad_up, w_up, preferred_element_type=jnp.float32)
    ).astype(jnp.bfloat16)
    return (row_grads, gate_grad, up_grad, down_grad)


def on_device(
    tokens,
    cotangent,
    routes,
    gates,
    plan,
    gate_values,
    up_values,
    down_values,
    gate_scales,
    up_scales,
    down_scales,
):
    tok_count, features = tokens.shape
    experts = lax.axis_size("expert")
    replicas = lax.axis_size("dp")
    capacity = 2
    half_bit = experts.bit_length() - 2
    expert_index = lax.axis_index("expert")
    numbers = jnp.arange(experts, dtype=jnp.int32)
    is_moved = jnp.sum(jnp.where(numbers == expert_index, plan, 0)) != expert_index
    own = (
        jnp.concatenate([gate_values, up_values, down_values], axis=0),
        jnp.concatenate([gate_scales, up_scales, down_scales], axis=0),
    )
    partner = swapped(own, "expert", half_bit)
    values, scales = (jnp.where(is_moved, b, a) for a, b in zip(own, partner))
    w_gate, w_up, w_down = (dequantize(values[i], scales[i]) for i in range(3))
    destination = jnp.take(plan, routes, axis=0)
    selected = slot_choice(destination, experts, capacity)
    dispatch = jnp.sum(selected.astype(jnp.int32), axis=1).reshape(
        tok_count, experts, capacity
    ).astype(jnp.bfloat16)
    slot_gate = jnp.einsum(
        "rkx,rk->rx", selected.astype(jnp.float32), gates.astype(jnp.float32)
    ).reshape(tok_count, experts, capacity).astype(jnp.bfloat16)
    zero = jnp.zeros_like(dispatch)
    pick = jnp.stack(
        [jnp.concatenate([dispatch, zero], axis=0), jnp.concatenate([zero, slot_gate], axis=0)], axis=0
    )
    sends = jnp.einsum(
        "srec,rd->csed", pick, jnp.concatenate([tokens, cotangent], axis=0),
        preferred_element_type=jnp.float32,
    ).astype(jnp.bfloat16)
    token_sum = jnp.zeros((tok_count, features), jnp.float32)
    sums = None
    for chunk in range(capacity):
        both = sends[chunk]
        arrived = lax.all_to_all(both, "expert", split_axis=1, concat_axis=1, tiled=True)
        gathered = lax.all_gather(arrived, "dp", axis=1, tiled=True)
        row_grads, gate_grad, up_grad, down_grad = expert_work(
            gathered[0], gathered[1], w_gate, w_up, w_down
        )
        part = (gate_grad, up_grad, down_grad)
        sums = part if sums is None else tuple(a + b for a, b in zip(sums, part))
        halves = 2 if chunk == capacity - 1 else 1
        width = features // halves
        pieces = []
        for half in range(halves):
            cols = slice(half * width, (half + 1) * width)
            summed_rows = lax.psum_scatter(
                row_grads[:, cols].reshape(replicas, experts, width), "dp", scatter_dimension=0, tiled=True
            )
            returned = lax.all_to_all(summed_rows[0], "expert", split_axis=0, concat_axis=0, tiled=True)
            pieces.append(jnp.einsum(
                "re,ed->rd", dispatch[:, :, chunk], returned, preferred_element_type=jnp.float32
            ))
        token_sum = token_sum + jnp.concatenate(pieces, axis=1)
    token_grads = token_sum.astype(jnp.bfloat16)
    gate_grad, up_grad, down_grad = (x.astype(jnp.bfloat16) for x in sums)
    return (token_grads, gate_grad[None], up_grad[None], down_grad[None])


def solution(mesh):
    return jax.shard_map(
        on_device,
        mesh=mesh,
        in_specs=(
            P(("dp", "expert"), None),
            P(("dp", "expert"), None),
            P(("dp", "expert"), None),
            P(("dp", "expert"), None),
            P(),
            P("expert", "dp", None),
            P("expert", "dp", None),
            P("expert", "dp", None),
            P("expert", "dp", None),
            P("expert", "dp", None),
            P("expert", "dp", None),
        ),
        out_specs=(
            P(("dp", "expert"), None),
            P("expert", "dp", None),
            P("expert", "dp", None),
            P("expert", "dp", None),
        ),
        check_vma=False,
    )
```
